32 devices in a mesh: energy: 4 (over z), atom: 8 (over y, x, core).
Axes of the slice: x: 2, y: 2, z: 4, core: 2. Of those that a mesh axis runs over, the one named last changes fastest.
Arguments:
- t_mats: bfloat16 [4, 16, 2048], P('energy', 'atom'), may hold values from -0.75 to 0.75
- struct_table: bfloat16 [4, 64, 2048], P('energy'), may hold values from -0.359375 to 0.359375
- zone_atoms: int32 [16, 64], P('atom'), may hold values from 0 to 15, as said below
- zone_size: int32 [16], P('atom'), may hold values from 32 to 64
- pair_index: int32 [16, 384], P('atom'), may hold values from 0 to 63
- zone_link: int32 [16, 384], P('atom'), may hold values from 0 to 63
- weights: float32 [4, 2], P('energy'), may hold values from -1 to 1
Outputs:
- green: float32 [16, 2048], P('atom')
The draws below stay inside these ranges and needn't reach their ends.
Inputs may be any that keep to these rules, and one draw needn't show every extreme that they name: Atom g is owned by index g // 2 of the atom axis; zone_atoms[g, 0] is g; the owner of every member of atom g's zone lies -4 to 3 steps from g's owner along the atom axis, counted around the axis, and both extreme offsets occur in every zone; members may repeat (periodic images).
All inputs are finite; a program needn't handle non-finite values.
Results may differ from the reference program's by a relative error of at most 0.003.
Values may be sent and summed in bfloat16 or wider, within the bound.
No kernel may reach another device: no remote copies, remote signals or barrier semaphores. Data moves between devices by JAX's collectives and lax.ppermute only.
A program may use at most 128 MiB of HBM per device.

```python
import jax
import jax.numpy as jnp
from jax import lax

L = 32
Z = 64
NB = 6
KTAB = 64
ITERS = 3
A_DEV = 2
ATOMS = 16
NE = 4
REACH = 4


def draw_zone_atoms(key, part):
    key_offset, key_local = jax.random.split(jax.random.fold_in(key, 7))
    owners_total = ATOMS // A_DEV
    offsets = jax.random.randint(key_offset, (ATOMS, Z), -REACH, REACH)
    offsets = offsets.at[:, 1].set(REACH - 1).at[:, 2].set(-REACH)
    local_ids = jax.random.randint(key_local, (ATOMS, Z), 0, A_DEV)
    owner_ids = jnp.arange(ATOMS, dtype=jnp.int32) // A_DEV
    member_ids = (owner_ids[:, None] + offsets) % owners_total * A_DEV + local_ids
    member_ids = member_ids.at[:, 0].set(jnp.arange(ATOMS, dtype=jnp.int32))
    return member_ids.astype(jnp.int32)


def plant(array, key, low, largest):
    longest = array.shape.index(max(array.shape))
    spots = []
    for shift in (0, 1):
        where = [jax.random.randint(jax.random.fold_in(key, axis), (), 0, length) for axis, length in enumerate(array.shape)]
        where[longest] = (where[longest] + shift) % array.shape[longest]
        spots.append(tuple(where))
    return array.at[spots[0]].set(low).at[spots[1]].set(largest)


def block_scale(own_key, extent, pieces, low, top_value):
    factor_of = 1.0
    for axis_at, blocks in pieces:
        steps = jax.random.uniform(jax.random.fold_in(jax.random.fold_in(own_key, 6), axis_at), (blocks,), jnp.float32, low / len(pieces), top_value / len(pieces))
        factor_of = factor_of * jnp.repeat(jnp.exp(steps), extent[axis_at] // blocks).reshape((-1,) + (1,) * (len(extent) - 1 - axis_at))
    return factor_of


def scatter_about(own_key, extent, deviation, most, cuts=(), kind=jnp.bfloat16):
    result = jax.random.normal(own_key, extent, jnp.float32) * deviation
    if len(cuts) > 0:
        result = block_scale(own_key, extent, cuts, -0.22, 0.18) * result
    return jnp.clip(result, min=-most, max=most).astype(kind)


def setup_inputs(seed: int = 0) -> dict:
    key_list = jax.random.split(jax.random.key(seed), 8)
    return {
        "t_mats": scatter_about(key_list[0], (NE, ATOMS, 2 * L * L), 0.125, 0.75, ((0, 4), (1, 8))),
        "struct_table": scatter_about(key_list[1], (NE, KTAB, 2 * L * L), 0.06, 0.359375, ((0, 4),)),
        "zone_atoms": draw_zone_atoms(jax.random.fold_in(key_list[7], 71), 0),
        "zone_size": plant(jax.random.randint(key_list[3], (ATOMS,), Z // 2, Z + 1), jax.random.fold_in(key_list[3], 1), Z // 2, Z).astype(jnp.int32),
        "pair_index": plant(jax.random.randint(key_list[4], (ATOMS, Z * NB), 0, KTAB), jax.random.fold_in(key_list[4], 1), 0, KTAB - 1).astype(jnp.int32),
        "zone_link": plant(jax.random.randint(key_list[5], (ATOMS, Z * NB), 0, Z), jax.random.fold_in(key_list[5], 1), 0, Z - 1).astype(jnp.int32),
        "weights": jnp.clip(jax.random.uniform(key_list[6], (NE, 2), jnp.float32, -1.0, 1.0) * block_scale(key_list[6], (NE, 2), ((0, 4),), -0.4, 0.0), -1.0, 1.0),
    }


def real_form(block):
    parts = block.reshape(block.shape[:-1] + (2, L, L))
    real_part = parts[..., 0, :, :]
    imag_part = parts[..., 1, :, :]
    top_rows = jnp.concatenate([real_part, -imag_part], axis=-1)
    bottom_rows = jnp.concatenate([imag_part, real_part], axis=-1)
    return jnp.concatenate([top_rows, bottom_rows], axis=-2)


def solve_zone(zone_block, table_real, pairs, links):
    t_real = real_form(zone_block).astype(jnp.float32)
    couplings = table_real[pairs.reshape(Z, NB)].astype(jnp.float32)
    link_table = links.reshape(Z, NB)
    start = jnp.zeros((Z, 2 * L, L), jnp.float32).at[0].set(t_real[0, :, :L])
    column = start
    for repeat in range(ITERS):
        near = column.astype(jnp.bfloat16).astype(jnp.float32)[link_table]
        coupled = jnp.einsum("anij,anjk->aik", couplings, near, precision=lax.Precision.HIGHEST)
        coupled = coupled.astype(jnp.bfloat16).astype(jnp.float32)
        column = jnp.einsum("aij,ajk->aik", t_real, coupled, precision=lax.Precision.HIGHEST) + start
    return column[0]


def reference(t_mats, struct_table, zone_atoms, zone_size, pair_index, zone_link, weights):
    present = jnp.arange(Z, dtype=jnp.int32)[None, :] < zone_size[:, None]

    def one_energy(inputs):
        t_energy, table_energy = inputs
        table_real = real_form(table_energy)

        def one_atom(atom_inputs):
            members, keep, pairs, links = atom_inputs
            zone_block = jnp.where(keep[:, None], t_energy[members], jnp.zeros((), jnp.bfloat16))
            return solve_zone(zone_block, table_real, pairs, links)

        return lax.map(one_atom, (zone_atoms, present, pair_index, zone_link))

    diagonal = lax.map(one_energy, (t_mats, struct_table))
    real_rows = diagonal[:, :, :L, :].reshape(NE, ATOMS, L * L)
    imag_rows = diagonal[:, :, L:, :].reshape(NE, ATOMS, L * L)
    w_real = weights[:, 0][:, None, None]
    w_imag = weights[:, 1][:, None, None]
    green_real = jnp.sum(w_real * real_rows - w_imag * imag_rows, axis=0)
    green_imag = jnp.sum(w_real * imag_rows + w_imag * real_rows, axis=0)
    return jnp.concatenate([green_real, green_imag], axis=-1)
```

```python
import jax
import jax.numpy as jnp
from jax import lax
from jax.sharding import PartitionSpec as P

L = 32
Z = 64
NB = 6


def real_form(block):
    parts = block.reshape(block.shape[:-1] + (2, L, L))
    real_part = parts[..., 0, :, :]
    imag_part = parts[..., 1, :, :]
    top_rows = jnp.concatenate([real_part, -imag_part], axis=-1)
    bottom_rows = jnp.concatenate([imag_part, real_part], axis=-1)
    return jnp.concatenate([top_rows, bottom_rows], axis=-2)


def take_rows(table, index):
    a_dev = index.shape[0]
    return jnp.take_along_axis(table, index.reshape(a_dev, -1), axis=1).reshape(index.shape)


def body(t_mats, struct_table, zone_atoms, zone_size, pair_index, zone_link, weights):
    e_dev, a_dev, block_flat = t_mats.shape
    window = lax.all_gather(t_mats, "atom", axis=1, tiled=True)

    coupling = jnp.arange(NB, dtype=jnp.int32)
    s2 = zone_link[:, :NB]
    s1 = take_rows(zone_link, s2[:, :, None] * NB + coupling)
    n1 = NB * NB
    slots = jnp.concatenate(
        [s1.reshape(a_dev, n1), s2, jnp.zeros((a_dev, 1), jnp.int32)], axis=1
    )
    spots = slots[:, :, None] * NB + coupling
    pairs = take_rows(pair_index, spots)
    links = take_rows(zone_link, spots)
    members = take_rows(zone_atoms, slots)
    present = slots < zone_size[:, None]

    t_block = jnp.where(
        present[None, :, :, None], window[:, members], jnp.zeros((), jnp.bfloat16)
    )
    t_real = real_form(t_block)
    g_real = real_form(struct_table[:, pairs])
    start_b = real_form(t_mats)[..., :L]
    start_f = start_b.astype(jnp.float32)
    is_zero = (slots == 0)[None, :, :, None, None]

    p1 = jnp.einsum(
        "easkij,eajc->easkic", g_real[:, :, :n1], start_b, preferred_element_type=jnp.float32
    )
    hit = (links[:, :n1] == 0)[None, :, :, :, None, None]
    coupled1 = jnp.sum(jnp.where(hit, p1, 0.0), axis=3).astype(jnp.bfloat16)
    col1 = jnp.einsum(
        "easij,easjc->easic", t_real[:, :, :n1], coupled1, preferred_element_type=jnp.float32
    ) + jnp.where(is_zero[:, :, :n1], start_f[:, :, None], 0.0)
    near2 = col1.astype(jnp.bfloat16).reshape(e_dev, a_dev, NB, NB, 2 * L, L)

    g2 = g_real[:, :, n1 : n1 + NB]
    coupled2 = jnp.einsum(
        "eamnij,eamnjc->eamic", g2, near2, preferred_element_type=jnp.float32
    ).astype(jnp.bfloat16)
    col2 = jnp.einsum(
        "eamij,eamjc->eamic", t_real[:, :, n1 : n1 + NB], coupled2,
        preferred_element_type=jnp.float32,
    ) + jnp.where(is_zero[:, :, n1 : n1 + NB], start_f[:, :, None], 0.0)
    near3 = col2.astype(jnp.bfloat16)

    coupled3 = jnp.einsum(
        "eanij,eanjc->eaic", g_real[:, :, n1 + NB], near3, preferred_element_type=jnp.float32
    ).astype(jnp.bfloat16)
    diagonal = jnp.einsum(
        "eaij,eajc->eaic", t_real[:, :, n1 + NB], coupled3, preferred_element_type=jnp.float32
    ) + start_f

    real_rows = diagonal[:, :, :L, :].reshape(e_dev, a_dev, L * L)
    imag_rows = diagonal[:, :, L:, :].reshape(e_dev, a_dev, L * L)
    w_real = weights[:, 0][:, None, None]
    w_imag = weights[:, 1][:, None, None]
    green_real = jnp.sum(w_real * real_rows - w_imag * imag_rows, axis=0)
    green_imag = jnp.sum(w_real * imag_rows + w_imag * real_rows, axis=0)
    local_green = jnp.concatenate([green_real, green_imag], axis=-1)
    return lax.psum(local_green, "energy")


def solution(mesh):
    return jax.shard_map(
        body,
        mesh=mesh,
        in_specs=(
            P("energy", "atom", None),
            P("energy", None, None),
            P("atom", None),
            P("atom"),
            P("atom", None),
            P("atom", None),
            P("energy", None),
        ),
        out_specs=P("atom", None),
        check_vma=False,
    )
```

```python
import jax
import jax.numpy as jnp
from jax import lax
from jax.experimental import pallas as pl
from jax.experimental.pallas import tpu as pltpu
from jax.sharding import PartitionSpec as P

L = 32
Z = 64
NB = 6


def real_form(block):
    parts = block.reshape(block.shape[:-1] + (2, L, L))
    real_part = parts[..., 0, :, :]
    imag_part = parts[..., 1, :, :]
    top_rows = jnp.concatenate([real_part, -imag_part], axis=-1)
    bottom_rows = jnp.concatenate([imag_part, real_part], axis=-1)
    return jnp.concatenate([top_rows, bottom_rows], axis=-2)


def zone_kernel(links, pairs, atoms, sizes, tab, tw, out, q, near2, near3):
    a_dev = out.shape[0]
    zl = L * 2
    n1 = NB * NB

    def block(ref, index):
        return ref[pl.ds(pl.multiple_of(index * zl, zl), zl), :]

    def dot(a, b):
        return jnp.dot(a, b, preferred_element_type=jnp.float32)

    for g in range(a_dev):
        base = g * Z * NB
        size = sizes[g]
        own = atoms[g * Z]
        start_b = block(tw, own)[:, :L]
        start_f = start_b.astype(jnp.float32)
        q[...] = dot(tab[...], start_b)

        def sweep1(i, carry):
            m = i // NB
            n = i - m * NB
            slot = links[base + links[base + m] * NB + n]
            acc = jnp.zeros((zl, L), jnp.float32)
            for k in range(NB):
                spot = base + slot * NB + k
                acc = acc + jnp.where(links[spot] == 0, block(q, pairs[spot]), 0.0)
            col = jnp.where(slot < size, dot(block(tw, atoms[g * Z + slot]), acc.astype(jnp.bfloat16)), 0.0)
            col = col + jnp.where(slot == 0, start_f, 0.0)
            near2[pl.ds(pl.multiple_of(i * zl, zl), zl), :] = col.astype(jnp.bfloat16)
            return carry

        lax.fori_loop(0, n1, sweep1, 0)

        for m in range(NB):
            slot = links[base + m]
            acc = jnp.zeros((zl, L), jnp.float32)
            for n in range(NB):
                acc = acc + dot(block(tab, pairs[base + slot * NB + n]), block(near2, m * NB + n))
            col = jnp.where(slot < size, dot(block(tw, atoms[g * Z + slot]), acc.astype(jnp.bfloat16)), 0.0)
            col = col + jnp.where(slot == 0, start_f, 0.0)
            near3[pl.ds(m * zl, zl), :] = col.astype(jnp.bfloat16)

        acc = jnp.zeros((zl, L), jnp.float32)
        for n in range(NB):
            acc = acc + dot(block(tab, pairs[base + n]), near3[pl.ds(n * zl, zl), :])
        out[g] = dot(block(tw, own), acc.astype(jnp.bfloat16)) + start_f


def body(t_mats, struct_table, zone_atoms, zone_size, pair_index, zone_link, weights):
    e_dev, a_dev, block_flat = t_mats.shape
    window = lax.all_gather(t_mats, "atom", axis=1, tiled=True)
    n_atoms = window.shape[1]
    k_tab = struct_table.shape[1]
    tab = real_form(struct_table[0]).reshape(k_tab * 2 * L, 2 * L)
    tw = real_form(window[0]).reshape(n_atoms * 2 * L, 2 * L)
    smem = pl.BlockSpec(memory_space=pltpu.SMEM)
    vmem = pl.BlockSpec(memory_space=pltpu.VMEM)
    diagonal = pl.pallas_call(
        zone_kernel,
        out_shape=jax.ShapeDtypeStruct((a_dev, 2 * L, L), jnp.float32),
        in_specs=[smem, smem, smem, smem, vmem, vmem],
        out_specs=vmem,
        scratch_shapes=[
            pltpu.VMEM((k_tab * 2 * L, L), jnp.float32),
            pltpu.VMEM((NB * NB * 2 * L, L), jnp.bfloat16),
            pltpu.VMEM((NB * 2 * L, L), jnp.bfloat16),
        ],
    )(zone_link.reshape(-1), pair_index.reshape(-1), zone_atoms.reshape(-1), zone_size, tab, tw)[None]

    real_rows = diagonal[:, :, :L, :].reshape(e_dev, a_dev, L * L)
    imag_rows = diagonal[:, :, L:, :].reshape(e_dev, a_dev, L * L)
    w_real = weights[:, 0][:, None, None]
    w_imag = weights[:, 1][:, None, None]
    green_real = jnp.sum(w_real * real_rows - w_imag * imag_rows, axis=0)
    green_imag = jnp.sum(w_real * imag_rows + w_imag * real_rows, axis=0)
    local_green = jnp.concatenate([green_real, green_imag], axis=-1)
    return lax.psum(local_green, "energy")


def solution(mesh):
    return jax.shard_map(
        body,
        mesh=mesh,
        in_specs=(
            P("energy", "atom", None),
            P("energy", None, None),
            P("atom", None),
            P("atom"),
            P("atom", None),
            P("atom", None),
            P("energy", None),
        ),
        out_specs=P("atom", None),
        check_vma=False,
    )
```

```python
import functools

import jax
import jax.numpy as jnp
from jax import lax
from jax.experimental import pallas as pl
from jax.experimental.pallas import tpu as pltpu
from jax.sharding import PartitionSpec as P

L = 32
Z = 64
NB = 6


def real_form(block):
    parts = block.reshape(block.shape[:-1] + (2, L, L))
    real_part = parts[..., 0, :, :]
    imag_part = parts[..., 1, :, :]
    top_rows = jnp.concatenate([real_part, -imag_part], axis=-1)
    bottom_rows = jnp.concatenate([imag_part, real_part], axis=-1)
    return jnp.concatenate([top_rows, bottom_rows], axis=-2)


def zone_kernel(links, pairs, atoms, sizes, wts, tab, tw, out, near2, near3, acc, flags):
    a_dev = out.shape[0]
    zl = L * 2
    n1 = NB * NB

    def rows(index):
        return pl.ds(pl.multiple_of(index * zl, zl), zl)

    def dot(a, b):
        return jnp.dot(a, b, preferred_element_type=jnp.float32)

    for g in range(a_dev):
        size = sizes[g]
        own = atoms[g, 0]
        start_b = tw[rows(own), :][:, :L]
        start_f = start_b.astype(jnp.float32)

        def finish(slot, index, dest):
            live = slot < size

            @pl.when(live)
            def _():
                col = dot(tw[rows(atoms[g, slot]), :], acc[...].astype(jnp.bfloat16))
                col = col + jnp.where(slot == 0, start_f, 0.0)
                dest[rows(index), :] = col.astype(jnp.bfloat16)

            @pl.when(jnp.logical_not(live))
            def _():
                dest[rows(index), :] = jnp.zeros((zl, L), jnp.bfloat16)

        def sweep1(i, carry):
            m = i // NB
            slot = links[g, links[g, m] * NB + i - m * NB]
            hits = jnp.int32(0)
            for k in range(NB):
                hits = hits + (links[g, slot * NB + k] == 0).astype(jnp.int32)
            live = hits > 0
            flags[i] = jnp.logical_or(live, slot == 0).astype(jnp.int32)

            @pl.when(live)
            def _():
                acc[...] = jnp.zeros((zl, L), jnp.float32)
                for k in range(NB):
                    spot = slot * NB + k

                    @pl.when(links[g, spot] == 0)
                    def _():
                        acc[...] += dot(tab[rows(pairs[g, spot]), :], start_b)

                finish(slot, i, near2)

            @pl.when(jnp.logical_not(live))
            def _():
                near2[rows(i), :] = jnp.where(slot == 0, start_b, jnp.zeros((), jnp.bfloat16))

            return carry

        lax.fori_loop(0, n1, sweep1, 0)

        for m in range(NB):
            slot = links[g, m]
            acc[...] = jnp.zeros((zl, L), jnp.float32)
            live = jnp.int32(0)
            for n in range(NB):
                i = m * NB + n

                @pl.when(flags[i] != 0)
                def _():
                    acc[...] += dot(tab[rows(pairs[g, slot * NB + n]), :], near2[rows(i), :])

                live = live | flags[i]
            flags[n1 + m] = jnp.logical_or(live != 0, slot == 0).astype(jnp.int32)

            @pl.when(live != 0)
            def _():
                finish(slot, m, near3)

            @pl.when(live == 0)
            def _():
                near3[rows(m), :] = jnp.where(slot == 0, start_b, jnp.zeros((), jnp.bfloat16))

        acc[...] = jnp.zeros((zl, L), jnp.float32)
        for n in range(NB):

            @pl.when(flags[n1 + n] != 0)
            def _():
                acc[...] += dot(tab[rows(pairs[g, n]), :], near3[rows(n), :])

        col = dot(tw[rows(own), :], acc[...].astype(jnp.bfloat16)) + start_f
        w_real = wts[0, 0]
        w_imag = wts[0, 1]
        out[g, :L, :] = w_real * col[:L] - w_imag * col[L:]
        out[g, L:, :] = w_real * col[L:] + w_imag * col[:L]


def xor_pairs(n, bit):
    return [(i, i ^ bit) for i in range(n)]


def gather_atoms(t_mats, n_axis):
    if n_axis & (n_axis - 1):
        return lax.all_gather(t_mats, "atom", axis=1, tiled=True)
    index = lax.axis_index("atom")
    blocks = t_mats
    bit = 1
    while bit < n_axis:
        other = lax.ppermute(blocks, "atom", xor_pairs(n_axis, bit))
        low = (index & bit) == 0
        blocks = jnp.where(
            low, jnp.concatenate([blocks, other], axis=1), jnp.concatenate([other, blocks], axis=1)
        )
        bit *= 2
    return blocks


def sum_energies(x, n_axis):
    if n_axis & (n_axis - 1):
        return lax.psum(x, "energy")
    bit = 1
    while bit < n_axis:
        x = x + lax.ppermute(x, "energy", xor_pairs(n_axis, bit))
        bit *= 2
    return x


def body(axis_sizes, t_mats, struct_table, zone_atoms, zone_size, pair_index, zone_link, weights):
    e_dev, a_dev, block_flat = t_mats.shape
    window = gather_atoms(t_mats, axis_sizes["atom"])
    n_atoms = window.shape[1]
    k_tab = struct_table.shape[1]
    tab = real_form(struct_table[0]).reshape(k_tab * 2 * L, 2 * L)
    tw = real_form(window[0]).reshape(n_atoms * 2 * L, 2 * L)
    smem = pl.BlockSpec(memory_space=pltpu.SMEM)
    vmem = pl.BlockSpec(memory_space=pltpu.VMEM)
    blocks = pl.pallas_call(
        zone_kernel,
        out_shape=jax.ShapeDtypeStruct((a_dev, 2 * L, L), jnp.float32),
        in_specs=[smem, smem, smem, smem, smem, vmem, vmem],
        out_specs=vmem,
        scratch_shapes=[
            pltpu.VMEM((NB * NB * 2 * L, L), jnp.bfloat16),
            pltpu.VMEM((NB * 2 * L, L), jnp.bfloat16),
            pltpu.VMEM((2 * L, L), jnp.float32),
            pltpu.SMEM((NB * NB + NB,), jnp.int32),
        ],
    )(zone_link, pair_index, zone_atoms, zone_size, weights, tab, tw)
    blocks = sum_energies(blocks, axis_sizes["energy"])
    return blocks.reshape(a_dev, 2, L * L).reshape(a_dev, 2 * L * L)


def solution(mesh):
    return jax.shard_map(
        functools.partial(body, dict(mesh.shape)),
        mesh=mesh,
        in_specs=(
            P("energy", "atom", None),
            P("energy", None, None),
            P("atom", None),
            P("atom"),
            P("atom", None),
            P("atom", None),
            P("energy", None),
        ),
        out_specs=P("atom", None),
        check_vma=False,
    )
```

```python
import functools

import jax
import jax.numpy as jnp
from jax import lax
from jax.experimental import pallas as pl
from jax.experimental.pallas import tpu as pltpu
from jax.sharding import PartitionSpec as P

L = 32
Z = 64
NB = 6


def real_form(block):
    parts = block.reshape(block.shape[:-1] + (2, L, L))
    real_part = parts[..., 0, :, :]
    imag_part = parts[..., 1, :, :]
    top_rows = jnp.concatenate([real_part, -imag_part], axis=-1)
    bottom_rows = jnp.concatenate([imag_part, real_part], axis=-1)
    return jnp.concatenate([top_rows, bottom_rows], axis=-2)


def zone_kernel(links, pairs, atoms, sizes, wts, reach, tab, tw, out, near3, acc, acc2, lists):
    a_dev = out.shape[0]
    zl = L * 2
    n1 = NB * NB

    def rows(index):
        return pl.ds(pl.multiple_of(index * zl, zl), zl)

    def dot(a, b):
        return jnp.dot(a, b, preferred_element_type=jnp.float32)

    zero_b = jnp.zeros((zl, L), jnp.bfloat16)
    zero_f = jnp.zeros((zl, L), jnp.float32)
    for g in range(a_dev):
        size = sizes[g]
        own = atoms[g, 0]
        start_b = tw[rows(own), :][:, :L]
        start_f = start_b.astype(jnp.float32)

        count = jnp.int32(0)
        for m in range(NB):
            base = links[g, m] * NB
            for n in range(NB):
                slot = links[g, base + n]
                lists[0, count] = m * NB + n
                lists[1, count] = slot
                count = count + jnp.logical_or(reach[g, slot] != 0, slot == 0).astype(jnp.int32)
        acc2[...] = jnp.zeros(acc2.shape, jnp.float32)
        for m in range(NB):
            lists[2, m] = jnp.int32(0)

        def sweep1(j, carry):
            i = lists[0, j]
            slot = lists[1, j]
            acc[...] = zero_f
            for k in range(NB):
                spot = slot * NB + k

                @pl.when(links[g, spot] == 0)
                def _():
                    acc[...] += dot(tab[rows(pairs[g, spot]), :], start_b)

            col = jnp.where(slot < size, dot(tw[rows(atoms[g, slot]), :], acc[...].astype(jnp.bfloat16)), 0.0)
            col = col + jnp.where(slot == 0, start_f, 0.0)
            m = i // NB
            parent = links[g, m]
            acc2[m] += dot(tab[rows(pairs[g, parent * NB + i - m * NB]), :], col.astype(jnp.bfloat16))
            lists[2, m] = jnp.int32(1)
            return carry

        lax.fori_loop(0, count, sweep1, 0)

        for m in range(NB):
            slot = links[g, m]
            live = jnp.logical_and(lists[2, m] != 0, slot < size)

            @pl.when(live)
            def _():
                col = dot(tw[rows(atoms[g, slot]), :], acc2[m].astype(jnp.bfloat16))
                col = col + jnp.where(slot == 0, start_f, 0.0)
                near3[rows(m), :] = col.astype(jnp.bfloat16)

            @pl.when(jnp.logical_not(live))
            def _():
                near3[rows(m), :] = jnp.where(slot == 0, start_b, zero_b)

        acc[...] = zero_f
        for n in range(NB):
            acc[...] += dot(tab[rows(pairs[g, n]), :], near3[rows(n), :])
        col = dot(tw[rows(own), :], acc[...].astype(jnp.bfloat16)) + start_f
        w_real = wts[0, 0]
        w_imag = wts[0, 1]
        out[g, :L, :] = w_real * col[:L] - w_imag * col[L:]
        out[g, L:, :] = w_real * col[L:] + w_imag * col[:L]


def xor_pairs(n, bit):
    return [(i, i ^ bit) for i in range(n)]


def gather_atoms(t_mats, n_axis):
    if n_axis & (n_axis - 1):
        return lax.all_gather(t_mats, "atom", axis=1, tiled=True)
    index = lax.axis_index("atom")
    blocks = t_mats
    bit = 1
    while bit < n_axis:
        other = lax.ppermute(blocks, "atom", xor_pairs(n_axis, bit))
        low = (index & bit) == 0
        blocks = jnp.where(
            low, jnp.concatenate([blocks, other], axis=1), jnp.concatenate([other, blocks], axis=1)
        )
        bit *= 2
    return blocks


def sum_energies(x, n_axis):
    if n_axis & (n_axis - 1):
        return lax.psum(x, "energy")
    bit = 1
    while bit < n_axis:
        x = x + lax.ppermute(x, "energy", xor_pairs(n_axis, bit))
        bit *= 2
    return x


def body(axis_sizes, t_mats, struct_table, zone_atoms, zone_size, pair_index, zone_link, weights):
    e_dev, a_dev, block_flat = t_mats.shape
    window = gather_atoms(t_mats, axis_sizes["atom"])
    n_atoms = window.shape[1]
    k_tab = struct_table.shape[1]
    tab = real_form(struct_table[0]).reshape(k_tab * 2 * L, 2 * L)
    tw = real_form(window[0]).reshape(n_atoms * 2 * L, 2 * L)
    z_slots = zone_atoms.shape[1]
    reach = jnp.any(zone_link.reshape(a_dev, z_slots, NB) == 0, axis=-1).astype(jnp.int32)
    smem = pl.BlockSpec(memory_space=pltpu.SMEM)
    vmem = pl.BlockSpec(memory_space=pltpu.VMEM)
    blocks = pl.pallas_call(
        zone_kernel,
        out_shape=jax.ShapeDtypeStruct((a_dev, 2 * L, L), jnp.float32),
        in_specs=[smem, smem, smem, smem, smem, smem, vmem, vmem],
        out_specs=vmem,
        scratch_shapes=[
            pltpu.VMEM((NB * 2 * L, L), jnp.bfloat16),
            pltpu.VMEM((2 * L, L), jnp.float32),
            pltpu.VMEM((NB, 2 * L, L), jnp.float32),
            pltpu.SMEM((3, NB * NB), jnp.int32),
        ],
    )(zone_link, pair_index, zone_atoms, zone_size, weights, reach, tab, tw)
    blocks = sum_energies(blocks, axis_sizes["energy"])
    return blocks.reshape(a_dev, 2, L * L).reshape(a_dev, 2 * L * L)


def solution(mesh):
    return jax.shard_map(
        functools.partial(body, dict(mesh.shape)),
        mesh=mesh,
        in_specs=(
            P("energy", "atom", None),
            P("energy", None, None),
            P("atom", None),
            P("atom"),
            P("atom", None),
            P("atom", None),
            P("energy", None),
        ),
        out_specs=P("atom", None),
        check_vma=False,
    )
```

```python
import functools

import jax
import jax.numpy as jnp
from jax import lax
from jax.experimental import pallas as pl
from jax.experimental.pallas import tpu as pltpu
from jax.sharding import PartitionSpec as P

L = 32
Z = 64
NB = 6


def real_form(block):
    parts = block.reshape(block.shape[:-1] + (2, L, L))
    real_part = parts[..., 0, :, :]
    imag_part = parts[..., 1, :, :]
    top_rows = jnp.concatenate([real_part, -imag_part], axis=-1)
    bottom_rows = jnp.concatenate([imag_part, real_part], axis=-1)
    return jnp.concatenate([top_rows, bottom_rows], axis=-2)


def zone_kernel(links, pairs, atoms, sizes, wts, reach, tab, tw, out, q, near3, acc, acc2, lists):
    a_dev = out.shape[0]
    zl = L * 2
    n1 = NB * NB
    width = 4
    spare = NB

    def rows(index):
        return pl.ds(pl.multiple_of(index * zl, zl), zl)

    def dot(a, b):
        return jnp.dot(a, b, preferred_element_type=jnp.float32)

    zero_b = jnp.zeros((zl, L), jnp.bfloat16)
    zero_f = jnp.zeros((zl, L), jnp.float32)
    for g in range(a_dev):
        size = sizes[g]
        own = atoms[g, 0]
        start_b = tw[rows(own), :][:, :L]
        start_f = start_b.astype(jnp.float32)
        q[...] = dot(tab[...], start_b)

        for j in range(lists.shape[1]):
            lists[0, j] = jnp.int32(0)
            lists[1, j] = jnp.int32(0)
            lists[2, j] = jnp.int32(spare)
        count = jnp.int32(0)
        for m in range(NB):
            base = links[g, m] * NB
            for n in range(NB):
                slot = links[g, base + n]
                lists[0, count] = slot
                lists[1, count] = pairs[g, base + n]
                lists[2, count] = jnp.int32(m)
                count = count + jnp.logical_or(reach[g, slot] != 0, slot == 0).astype(jnp.int32)
            lists[3, m] = jnp.int32(0)
        acc2[...] = jnp.zeros(acc2.shape, jnp.float32)

        def sweep1(c, carry):
            parts = []
            for u in range(width):
                j = c * width + u
                slot = lists[0, j]
                coupled = zero_f
                for k in range(NB):
                    spot = slot * NB + k
                    coupled = coupled + jnp.where(links[g, spot] == 0, q[rows(pairs[g, spot]), :], 0.0)
                col = jnp.where(slot < size, dot(tw[rows(atoms[g, slot]), :], coupled.astype(jnp.bfloat16)), 0.0)
                col = col + jnp.where(slot == 0, start_f, 0.0)
                parts.append(dot(tab[rows(lists[1, j]), :], col.astype(jnp.bfloat16)))
            for u in range(width):
                j = c * width + u
                m = lists[2, j]
                acc2[m] += parts[u]
                lists[3, m] = jnp.int32(1)
            return carry

        lax.fori_loop(0, (count + width - 1) // width, sweep1, 0)

        for m in range(NB):
            slot = links[g, m]
            live = jnp.logical_and(lists[3, m] != 0, slot < size)

            @pl.when(live)
            def _():
                col = dot(tw[rows(atoms[g, slot]), :], acc2[m].astype(jnp.bfloat16))
                col = col + jnp.where(slot == 0, start_f, 0.0)
                near3[rows(m), :] = col.astype(jnp.bfloat16)

            @pl.when(jnp.logical_not(live))
            def _():
                near3[rows(m), :] = jnp.where(slot == 0, start_b, zero_b)

        acc[...] = zero_f
        for n in range(NB):
            acc[...] += dot(tab[rows(pairs[g, n]), :], near3[rows(n), :])
        col = dot(tw[rows(own), :], acc[...].astype(jnp.bfloat16)) + start_f
        w_real = wts[0, 0]
        w_imag = wts[0, 1]
        out[g, :L, :] = w_real * col[:L] - w_imag * col[L:]
        out[g, L:, :] = w_real * col[L:] + w_imag * col[:L]


def xor_pairs(n, bit):
    return [(i, i ^ bit) for i in range(n)]


def gather_atoms(t_mats, n_axis):
    if n_axis & (n_axis - 1):
        return lax.all_gather(t_mats, "atom", axis=1, tiled=True)
    index = lax.axis_index("atom")
    blocks = t_mats
    bit = 1
    while bit < n_axis:
        other = lax.ppermute(blocks, "atom", xor_pairs(n_axis, bit))
        low = (index & bit) == 0
        blocks = jnp.where(
            low, jnp.concatenate([blocks, other], axis=1), jnp.concatenate([other, blocks], axis=1)
        )
        bit *= 2
    return blocks


def sum_energies(x, n_axis):
    if n_axis & (n_axis - 1):
        return lax.psum(x, "energy")
    bit = 1
    while bit < n_axis:
        x = x + lax.ppermute(x, "energy", xor_pairs(n_axis, bit))
        bit *= 2
    return x


def body(axis_sizes, t_mats, struct_table, zone_atoms, zone_size, pair_index, zone_link, weights):
    e_dev, a_dev, block_flat = t_mats.shape
    window = gather_atoms(t_mats, axis_sizes["atom"])
    n_atoms = window.shape[1]
    k_tab = struct_table.shape[1]
    tab = real_form(struct_table[0]).reshape(k_tab * 2 * L, 2 * L)
    tw = real_form(window[0]).reshape(n_atoms * 2 * L, 2 * L)
    z_slots = zone_atoms.shape[1]
    reach = jnp.any(zone_link.reshape(a_dev, z_slots, NB) == 0, axis=-1).astype(jnp.int32)
    smem = pl.BlockSpec(memory_space=pltpu.SMEM)
    vmem = pl.BlockSpec(memory_space=pltpu.VMEM)
    blocks = pl.pallas_call(
        zone_kernel,
        out_shape=jax.ShapeDtypeStruct((a_dev, 2 * L, L), jnp.float32),
        in_specs=[smem, smem, smem, smem, smem, smem, vmem, vmem],
        out_specs=vmem,
        scratch_shapes=[
            pltpu.VMEM((k_tab * 2 * L, L), jnp.float32),
            pltpu.VMEM((NB * 2 * L, L), jnp.bfloat16),
            pltpu.VMEM((2 * L, L), jnp.float32),
            pltpu.VMEM((NB + 1, 2 * L, L), jnp.float32),
            pltpu.SMEM((4, NB * NB + 4), jnp.int32),
        ],
    )(zone_link, pair_index, zone_atoms, zone_size, weights, reach, tab, tw)
    blocks = sum_energies(blocks, axis_sizes["energy"])
    return blocks.reshape(a_dev, 2, L * L).reshape(a_dev, 2 * L * L)


def solution(mesh):
    return jax.shard_map(
        functools.partial(body, dict(mesh.shape)),
        mesh=mesh,
        in_specs=(
            P("energy", "atom", None),
            P("energy", None, None),
            P("atom", None),
            P("atom"),
            P("atom", None),
            P("atom", None),
            P("energy", None),
        ),
        out_specs=P("atom", None),
        check_vma=False,
    )
```

```python
import functools

import jax
import jax.numpy as jnp
from jax import lax
from jax.experimental import pallas as pl
from jax.experimental.pallas import tpu as pltpu
from jax.sharding import PartitionSpec as P

L = 32
Z = 64
NB = 6


def real_form(block):
    parts = block.reshape(block.shape[:-1] + (2, L, L))
    real_part = parts[..., 0, :, :]
    imag_part = parts[..., 1, :, :]
    top_rows = jnp.concatenate([real_part, -imag_part], axis=-1)
    bottom_rows = jnp.concatenate([imag_part, real_part], axis=-1)
    return jnp.concatenate([top_rows, bottom_rows], axis=-2)


def zone_kernel(links, pairs, atoms, sizes, wts, reach, tab, tw, out, q, near3, acc, acc2, lists):
    a_dev = out.shape[0]
    zl = L * 2
    n1 = NB * NB
    width = 4
    spare = NB

    def rows(index):
        return pl.ds(pl.multiple_of(index * zl, zl), zl)

    def dot(a, b):
        return jnp.dot(a, b, preferred_element_type=jnp.float32)

    zero_b = jnp.zeros((zl, L), jnp.bfloat16)
    zero_f = jnp.zeros((zl, L), jnp.float32)
    for g in range(a_dev):
        size = sizes[g]
        own = atoms[g, 0]
        start_b = tw[rows(own), :][:, :L]
        start_f = start_b.astype(jnp.float32)
        q[...] = dot(tab[...], start_b)

        for j in range(lists.shape[1]):
            lists[0, j] = jnp.int32(0)
            lists[1, j] = jnp.int32(0)
            lists[2, j] = jnp.int32(spare)
        count = jnp.int32(0)
        for m in range(NB):
            base = links[g, m] * NB
            for n in range(NB):
                slot = links[g, base + n]
                lists[0, count] = slot
                lists[1, count] = pairs[g, base + n]
                lists[2, count] = jnp.int32(m)
                count = count + jnp.logical_or(reach[g, slot] != 0, slot == 0).astype(jnp.int32)
            lists[3, m] = jnp.int32(0)
        acc2[...] = jnp.zeros(acc2.shape, jnp.float32)

        def sweep1(c, carry):
            parts = []
            for u in range(width):
                j = c * width + u
                slot = lists[0, j]
                coupled = zero_f
                for k in range(NB):
                    spot = slot * NB + k
                    coupled = coupled + jnp.where(links[g, spot] == 0, q[rows(pairs[g, spot]), :], 0.0)
                col = jnp.where(slot < size, dot(tw[rows(atoms[g, slot]), :], coupled.astype(jnp.bfloat16)), 0.0)
                col = col + jnp.where(slot == 0, start_f, 0.0)
                parts.append(dot(tab[rows(lists[1, j]), :], col.astype(jnp.bfloat16)))
            for u in range(width):
                j = c * width + u
                m = lists[2, j]
                acc2[m] += parts[u]
                lists[3, m] = jnp.int32(1)
            return carry

        lax.fori_loop(0, (count + width - 1) // width, sweep1, 0)

        for m in range(NB):
            slot = links[g, m]
            live = jnp.logical_and(lists[3, m] != 0, slot < size)

            @pl.when(live)
            def _():
                col = dot(tw[rows(atoms[g, slot]), :], acc2[m].astype(jnp.bfloat16))
                col = col + jnp.where(slot == 0, start_f, 0.0)
                near3[rows(m), :] = col.astype(jnp.bfloat16)

            @pl.when(jnp.logical_not(live))
            def _():
                near3[rows(m), :] = jnp.where(slot == 0, start_b, zero_b)

        acc[...] = zero_f
        for n in range(NB):
            acc[...] += dot(tab[rows(pairs[g, n]), :], near3[rows(n), :])
        col = dot(tw[rows(own), :], acc[...].astype(jnp.bfloat16)) + start_f
        w_real = wts[0, 0]
        w_imag = wts[0, 1]
        out[g, :L, :] = w_real * col[:L] - w_imag * col[L:]
        out[g, L:, :] = w_real * col[L:] + w_imag * col[:L]


def xor_pairs(n, bit):
    return [(i, i ^ bit) for i in range(n)]


def gather_atoms(t_mats, n_axis, later):
    if n_axis & (n_axis - 1):
        return lax.all_gather(t_mats, "atom", axis=1, tiled=True), later
    index = lax.axis_index("atom")
    blocks = t_mats
    bit = 1
    while bit < n_axis:
        other = lax.ppermute(blocks, "atom", xor_pairs(n_axis, bit))
        if bit <= 2:
            other, later[bit - 1] = lax.optimization_barrier((other, later[bit - 1]))
        low = (index & bit) == 0
        blocks = jnp.where(
            low, jnp.concatenate([blocks, other], axis=1), jnp.concatenate([other, blocks], axis=1)
        )
        bit *= 2
    return blocks, later


def sum_energies(x, n_axis):
    if n_axis & (n_axis - 1):
        return lax.psum(x, "energy")
    bit = 1
    while bit < n_axis:
        x = x + lax.ppermute(x, "energy", xor_pairs(n_axis, bit))
        bit *= 2
    return x


def body(axis_sizes, t_mats, struct_table, zone_atoms, zone_size, pair_index, zone_link, weights):
    e_dev, a_dev, block_flat = t_mats.shape
    window, (table, zone_link) = gather_atoms(t_mats, axis_sizes["atom"], [struct_table, zone_link])
    n_atoms = window.shape[1]
    k_tab = struct_table.shape[1]
    tab = real_form(table[0]).reshape(k_tab * 2 * L, 2 * L)
    tw = real_form(window[0]).reshape(n_atoms * 2 * L, 2 * L)
    z_slots = zone_atoms.shape[1]
    reach = jnp.any(zone_link.reshape(a_dev, z_slots, NB) == 0, axis=-1).astype(jnp.int32)
    smem = pl.BlockSpec(memory_space=pltpu.SMEM)
    vmem = pl.BlockSpec(memory_space=pltpu.VMEM)
    blocks = pl.pallas_call(
        zone_kernel,
        out_shape=jax.ShapeDtypeStruct((a_dev, 2 * L, L), jnp.float32),
        in_specs=[smem, smem, smem, smem, smem, smem, vmem, vmem],
        out_specs=vmem,
        scratch_shapes=[
            pltpu.VMEM((k_tab * 2 * L, L), jnp.float32),
            pltpu.VMEM((NB * 2 * L, L), jnp.bfloat16),
            pltpu.VMEM((2 * L, L), jnp.float32),
            pltpu.VMEM((NB + 1, 2 * L, L), jnp.float32),
            pltpu.SMEM((4, NB * NB + 4), jnp.int32),
        ],
    )(zone_link, pair_index, zone_atoms, zone_size, weights, reach, tab, tw)
    blocks = sum_energies(blocks, axis_sizes["energy"])
    return blocks.reshape(a_dev, 2, L * L).reshape(a_dev, 2 * L * L)


def solution(mesh):
    return jax.shard_map(
        functools.partial(body, dict(mesh.shape)),
        mesh=mesh,
        in_specs=(
            P("energy", "atom", None),
            P("energy", None, None),
            P("atom", None),
            P("atom"),
            P("atom", None),
            P("atom", None),
            P("energy", None),
        ),
        out_specs=P("atom", None),
        check_vma=False,
    )
```

```python
import functools

import jax
import jax.numpy as jnp
from jax import lax
from jax.experimental import pallas as pl
from jax.experimental.pallas import tpu as pltpu
from jax.sharding import PartitionSpec as P

L = 32
Z = 64
NB = 6


def real_form(block):
    parts = block.reshape(block.shape[:-1] + (2, L, L))
    real_part = parts[..., 0, :, :]
    imag_part = parts[..., 1, :, :]
    top_rows = jnp.concatenate([real_part, -imag_part], axis=-1)
    bottom_rows = jnp.concatenate([imag_part, real_part], axis=-1)
    return jnp.concatenate([top_rows, bottom_rows], axis=-2)


def zone_kernel(links, pairs, atoms, sizes, wts, reach, tab, tw, out, q, near3, acc, acc2, lists):
    a_dev = out.shape[0]
    zl = L * 2
    n1 = NB * NB
    width = 4
    spare = NB

    def rows(index):
        return pl.ds(pl.multiple_of(index * zl, zl), zl)

    def dot(a, b):
        return jnp.dot(a, b, preferred_element_type=jnp.float32)

    zero_b = jnp.zeros((zl, L), jnp.bfloat16)
    zero_f = jnp.zeros((zl, L), jnp.float32)
    for g in range(a_dev):
        size = sizes[g]
        own = atoms[g, 0]
        start_b = tw[rows(own), :][:, :L]
        start_f = start_b.astype(jnp.float32)
        q[...] = dot(tab[...], start_b)

        for j in range(lists.shape[1]):
            lists[0, j] = jnp.int32(0)
            lists[1, j] = jnp.int32(0)
            lists[2, j] = jnp.int32(spare)
        count = jnp.int32(0)
        for m in range(NB):
            base = links[g, m] * NB
            for n in range(NB):
                slot = links[g, base + n]
                lists[0, count] = slot
                lists[1, count] = pairs[g, base + n]
                lists[2, count] = jnp.int32(m)
                count = count + jnp.logical_or(reach[g, slot] != 0, slot == 0).astype(jnp.int32)
            lists[3, m] = jnp.int32(0)
        acc2[...] = jnp.zeros(acc2.shape, jnp.float32)

        def sweep1(c, carry):
            parts = []
            for u in range(width):
                j = c * width + u
                slot = lists[0, j]
                coupled = zero_f
                for k in range(NB):
                    spot = slot * NB + k
                    coupled = coupled + jnp.where(links[g, spot] == 0, q[rows(pairs[g, spot]), :], 0.0)
                col = jnp.where(slot < size, dot(tw[rows(atoms[g, slot]), :], coupled.astype(jnp.bfloat16)), 0.0)
                col = col + jnp.where(slot == 0, start_f, 0.0)
                parts.append(dot(tab[rows(lists[1, j]), :], col.astype(jnp.bfloat16)))
            for u in range(width):
                j = c * width + u
                m = lists[2, j]
                acc2[m] += parts[u]
                lists[3, m] = jnp.int32(1)
            return carry

        lax.fori_loop(0, (count + width - 1) // width, sweep1, 0)

        for m in range(NB):
            slot = links[g, m]
            live = jnp.logical_and(lists[3, m] != 0, slot < size)

            @pl.when(live)
            def _():
                col = dot(tw[rows(atoms[g, slot]), :], acc2[m].astype(jnp.bfloat16))
                col = col + jnp.where(slot == 0, start_f, 0.0)
                near3[rows(m), :] = col.astype(jnp.bfloat16)

            @pl.when(jnp.logical_not(live))
            def _():
                near3[rows(m), :] = jnp.where(slot == 0, start_b, zero_b)

        acc[...] = zero_f
        for n in range(NB):
            acc[...] += dot(tab[rows(pairs[g, n]), :], near3[rows(n), :])
        col = dot(tw[rows(own), :], acc[...].astype(jnp.bfloat16)) + start_f
        w_real = wts[0, 0]
        w_imag = wts[0, 1]
        green = jnp.concatenate(
            [w_real * col[:L] - w_imag * col[L:], w_real * col[L:] + w_imag * col[:L]], axis=0
        )
        out[g] = green.reshape(out.shape[1:])


def xor_pairs(n, bit):
    return [(i, i ^ bit) for i in range(n)]


def gather_atoms(t_mats, n_axis, later):
    if n_axis & (n_axis - 1):
        return lax.all_gather(t_mats, "atom", axis=1, tiled=True), later
    index = lax.axis_index("atom")
    blocks = t_mats
    bit = 1
    while bit < n_axis:
        other = lax.ppermute(blocks, "atom", xor_pairs(n_axis, bit))
        if bit <= 2:
            other, later[bit - 1] = lax.optimization_barrier((other, later[bit - 1]))
        low = (index & bit) == 0
        blocks = jnp.where(
            low, jnp.concatenate([blocks, other], axis=1), jnp.concatenate([other, blocks], axis=1)
        )
        bit *= 2
    return blocks, later


def sum_energies(x, n_axis):
    if n_axis & (n_axis - 1):
        return lax.psum(x, "energy")
    bit = 1
    while bit < n_axis:
        x = x + lax.ppermute(x, "energy", xor_pairs(n_axis, bit))
        bit *= 2
    return x


def body(axis_sizes, t_mats, struct_table, zone_atoms, zone_size, pair_index, zone_link, weights):
    e_dev, a_dev, block_flat = t_mats.shape
    window, (table, zone_link) = gather_atoms(t_mats, axis_sizes["atom"], [struct_table, zone_link])
    n_atoms = window.shape[1]
    k_tab = struct_table.shape[1]
    tab = real_form(table[0]).reshape(k_tab * 2 * L, 2 * L)
    tw = real_form(window[0]).reshape(n_atoms * 2 * L, 2 * L)
    z_slots = zone_atoms.shape[1]
    reach = jnp.any(zone_link.reshape(a_dev, z_slots, NB) == 0, axis=-1).astype(jnp.int32)
    smem = pl.BlockSpec(memory_space=pltpu.SMEM)
    vmem = pl.BlockSpec(memory_space=pltpu.VMEM)
    blocks = pl.pallas_call(
        zone_kernel,
        out_shape=jax.ShapeDtypeStruct((a_dev, 2 * L * L // 128, 128), jnp.float32),
        in_specs=[smem, smem, smem, smem, smem, smem, vmem, vmem],
        out_specs=vmem,
        scratch_shapes=[
            pltpu.VMEM((k_tab * 2 * L, L), jnp.float32),
            pltpu.VMEM((NB * 2 * L, L), jnp.bfloat16),
            pltpu.VMEM((2 * L, L), jnp.float32),
            pltpu.VMEM((NB + 1, 2 * L, L), jnp.float32),
            pltpu.SMEM((4, NB * NB + 4), jnp.int32),
        ],
    )(zone_link, pair_index, zone_atoms, zone_size, weights, reach, tab, tw)
    blocks = sum_energies(blocks, axis_sizes["energy"])
    return blocks.reshape(a_dev, 2 * L * L)


def solution(mesh):
    return jax.shard_map(
        functools.partial(body, dict(mesh.shape)),
        mesh=mesh,
        in_specs=(
            P("energy", "atom", None),
            P("energy", None, None),
            P("atom", None),
            P("atom"),
            P("atom", None),
            P("atom", None),
            P("energy", None),
        ),
        out_specs=P("atom", None),
        check_vma=False,
    )
```

```python
import functools

import jax
import jax.numpy as jnp
from jax import lax
from jax.experimental import pallas as pl
from jax.experimental.pallas import tpu as pltpu
from jax.sharding import PartitionSpec as P

L = 32
Z = 64
NB = 6


def real_form(block):
    parts = block.reshape(block.shape[:-1] + (2, L, L))
    real_part = parts[..., 0, :, :]
    imag_part = parts[..., 1, :, :]
    top_rows = jnp.concatenate([real_part, -imag_part], axis=-1)
    bottom_rows = jnp.concatenate([imag_part, real_part], axis=-1)
    return jnp.concatenate([top_rows, bottom_rows], axis=-2)


def zone_kernel(links, pairs, atoms, sizes, wts, reach, tab, tw, out, q, near3, acc, acc2, lists):
    a_dev = out.shape[0]
    zl = L * 2
    n1 = NB * NB
    width = 8
    spare = NB

    def rows(index):
        return pl.ds(pl.multiple_of(index * zl, zl), zl)

    def dot(a, b):
        return jnp.dot(a, b, preferred_element_type=jnp.float32)

    zero_b = jnp.zeros((zl, L), jnp.bfloat16)
    zero_f = jnp.zeros((zl, L), jnp.float32)
    for g in range(a_dev):
        size = sizes[g]
        own = atoms[g, 0]
        start_b = tw[rows(own), :][:, :L]
        start_f = start_b.astype(jnp.float32)
        q[...] = dot(tab[...], start_b)

        for j in range(lists.shape[1]):
            lists[0, j] = jnp.int32(0)
            lists[1, j] = jnp.int32(0)
            lists[2, j] = jnp.int32(spare)
        count = jnp.int32(0)
        for m in range(NB):
            base = links[g, m] * NB
            for n in range(NB):
                slot = links[g, base + n]
                lists[0, count] = slot
                lists[1, count] = pairs[g, base + n]
                lists[2, count] = jnp.int32(m)
                count = count + jnp.logical_or(reach[g, slot] != 0, slot == 0).astype(jnp.int32)
            lists[3, m] = jnp.int32(0)
        acc2[...] = jnp.zeros(acc2.shape, jnp.float32)

        def sweep1(c, carry):
            parts = []
            for u in range(width):
                j = c * width + u
                slot = lists[0, j]
                coupled = zero_f
                for k in range(NB):
                    spot = slot * NB + k
                    coupled = coupled + jnp.where(links[g, spot] == 0, q[rows(pairs[g, spot]), :], 0.0)
                col = jnp.where(slot < size, dot(tw[rows(atoms[g, slot]), :], coupled.astype(jnp.bfloat16)), 0.0)
                col = col + jnp.where(slot == 0, start_f, 0.0)
                parts.append(dot(tab[rows(lists[1, j]), :], col.astype(jnp.bfloat16)))
            for u in range(width):
                j = c * width + u
                m = lists[2, j]
                acc2[m] += parts[u]
                lists[3, m] = jnp.int32(1)
            return carry

        lax.fori_loop(0, (count + width - 1) // width, sweep1, 0)

        for m in range(NB):
            slot = links[g, m]
            live = jnp.logical_and(lists[3, m] != 0, slot < size)

            @pl.when(live)
            def _():
                col = dot(tw[rows(atoms[g, slot]), :], acc2[m].astype(jnp.bfloat16))
                col = col + jnp.where(slot == 0, start_f, 0.0)
                near3[rows(m), :] = col.astype(jnp.bfloat16)

            @pl.when(jnp.logical_not(live))
            def _():
                near3[rows(m), :] = jnp.where(slot == 0, start_b, zero_b)

        acc[...] = zero_f
        for n in range(NB):
            acc[...] += dot(tab[rows(pairs[g, n]), :], near3[rows(n), :])
        col = dot(tw[rows(own), :], acc[...].astype(jnp.bfloat16)) + start_f
        w_real = wts[0, 0]
        w_imag = wts[0, 1]
        green = jnp.concatenate(
            [w_real * col[:L] - w_imag * col[L:], w_real * col[L:] + w_imag * col[:L]], axis=0
        )
        out[g] = green.reshape(out.shape[1:])


def xor_pairs(n, bit):
    return [(i, i ^ bit) for i in range(n)]


def gather_atoms(t_mats, n_axis, later):
    if n_axis & (n_axis - 1):
        return lax.all_gather(t_mats, "atom", axis=1, tiled=True), later
    index = lax.axis_index("atom")
    blocks = t_mats
    bit = 1
    while bit < n_axis:
        other = lax.ppermute(blocks, "atom", xor_pairs(n_axis, bit))
        if bit <= 2:
            other, later[bit - 1] = lax.optimization_barrier((other, later[bit - 1]))
        low = (index & bit) == 0
        blocks = jnp.where(
            low, jnp.concatenate([blocks, other], axis=1), jnp.concatenate([other, blocks], axis=1)
        )
        bit *= 2
    return blocks, later


def sum_energies(x, n_axis):
    if n_axis & (n_axis - 1):
        return lax.psum(x, "energy")
    bit = 1
    while bit < n_axis:
        x = x + lax.ppermute(x, "energy", xor_pairs(n_axis, bit))
        bit *= 2
    return x


def body(axis_sizes, t_mats, struct_table, zone_atoms, zone_size, pair_index, zone_link, weights):
    e_dev, a_dev, block_flat = t_mats.shape
    window, (table, zone_link) = gather_atoms(t_mats, axis_sizes["atom"], [struct_table, zone_link])
    n_atoms = window.shape[1]
    k_tab = struct_table.shape[1]
    tab = real_form(table[0]).reshape(k_tab * 2 * L, 2 * L)
    tw = real_form(window[0]).reshape(n_atoms * 2 * L, 2 * L)
    z_slots = zone_atoms.shape[1]
    reach = jnp.any(zone_link.reshape(a_dev, z_slots, NB) == 0, axis=-1).astype(jnp.int32)
    smem = pl.BlockSpec(memory_space=pltpu.SMEM)
    vmem = pl.BlockSpec(memory_space=pltpu.VMEM)
    blocks = pl.pallas_call(
        zone_kernel,
        out_shape=jax.ShapeDtypeStruct((a_dev, 2 * L * L // 128, 128), jnp.float32),
        in_specs=[smem, smem, smem, smem, smem, smem, vmem, vmem],
        out_specs=vmem,
        scratch_shapes=[
            pltpu.VMEM((k_tab * 2 * L, L), jnp.float32),
            pltpu.VMEM((NB * 2 * L, L), jnp.bfloat16),
            pltpu.VMEM((2 * L, L), jnp.float32),
            pltpu.VMEM((NB + 1, 2 * L, L), jnp.float32),
            pltpu.SMEM((4, NB * NB + 8), jnp.int32),
        ],
    )(zone_link, pair_index, zone_atoms, zone_size, weights, reach, tab, tw)
    blocks = sum_energies(blocks, axis_sizes["energy"])
    return blocks.reshape(a_dev, 2 * L * L)


def solution(mesh):
    return jax.shard_map(
        functools.partial(body, dict(mesh.shape)),
        mesh=mesh,
        in_specs=(
            P("energy", "atom", None),
            P("energy", None, None),
            P("atom", None),
            P("atom"),
            P("atom", None),
            P("atom", None),
            P("energy", None),
        ),
        out_specs=P("atom", None),
        check_vma=False,
    )
```

```python
import functools

import jax
import jax.numpy as jnp
from jax import lax
from jax.experimental import pallas as pl
from jax.experimental.pallas import tpu as pltpu
from jax.sharding import PartitionSpec as P

L = 32
Z = 64
NB = 6


def real_form(block):
    parts = block.reshape(block.shape[:-1] + (2, L, L))
    real_part = parts[..., 0, :, :]
    imag_part = parts[..., 1, :, :]
    top_rows = jnp.concatenate([real_part, -imag_part], axis=-1)
    bottom_rows = jnp.concatenate([imag_part, real_part], axis=-1)
    return jnp.concatenate([top_rows, bottom_rows], axis=-2)


def zone_kernel(links, pairs, atoms, sizes, wts, reach, tab, tw, out, q, near3, acc, acc2, lists):
    a_dev = out.shape[0]
    zl = L * 2
    n1 = NB * NB
    width = 4
    spare = NB

    def rows(index):
        return pl.ds(pl.multiple_of(index * zl, zl), zl)

    def dot(a, b):
        return jnp.dot(a, b, preferred_element_type=jnp.float32)

    zero_b = jnp.zeros((zl, L), jnp.bfloat16)
    zero_f = jnp.zeros((zl, L), jnp.float32)
    sizes_g = [sizes[g] for g in range(a_dev)]
    starts_b = []
    counts = []
    for g in range(a_dev):
        start_b = tw[rows(atoms[g, 0]), :][:, :L]
        starts_b.append(start_b)
        q[g] = dot(tab[...], start_b)
        for j in range(lists.shape[2]):
            lists[g, 0, j] = jnp.int32(0)
            lists[g, 1, j] = jnp.int32(0)
            lists[g, 2, j] = jnp.int32(spare)
        count = jnp.int32(0)
        for m in range(NB):
            base = links[g, m] * NB
            for n in range(NB):
                slot = links[g, base + n]
                lists[g, 0, count] = slot
                lists[g, 1, count] = pairs[g, base + n]
                lists[g, 2, count] = jnp.int32(m)
                count = count + jnp.logical_or(reach[g, slot] != 0, slot == 0).astype(jnp.int32)
            lists[g, 3, m] = jnp.int32(0)
        counts.append(count)
    acc2[...] = jnp.zeros(acc2.shape, jnp.float32)

    def sweep1(c, carry):
        parts = []
        for g in range(a_dev):
            for u in range(width):
                j = c * width + u
                slot = lists[g, 0, j]
                coupled = zero_f
                for k in range(NB):
                    spot = slot * NB + k
                    coupled = coupled + jnp.where(links[g, spot] == 0, q[g, rows(pairs[g, spot]), :], 0.0)
                col = jnp.where(slot < sizes_g[g], dot(tw[rows(atoms[g, slot]), :], coupled.astype(jnp.bfloat16)), 0.0)
                col = col + jnp.where(slot == 0, starts_b[g].astype(jnp.float32), 0.0)
                parts.append(dot(tab[rows(lists[g, 1, j]), :], col.astype(jnp.bfloat16)))
        for g in range(a_dev):
            for u in range(width):
                j = c * width + u
                m = lists[g, 2, j]
                acc2[g, m] += parts[g * width + u]
                lists[g, 3, m] = jnp.int32(1)
        return carry

    most = counts[0]
    for count in counts[1:]:
        most = jnp.maximum(most, count)
    lax.fori_loop(0, (most + width - 1) // width, sweep1, 0)

    for g in range(a_dev):
        size = sizes_g[g]
        own = atoms[g, 0]
        start_b = starts_b[g]
        start_f = start_b.astype(jnp.float32)
        for m in range(NB):
            slot = links[g, m]
            live = jnp.logical_and(lists[g, 3, m] != 0, slot < size)

            @pl.when(live)
            def _():
                col = dot(tw[rows(atoms[g, slot]), :], acc2[g, m].astype(jnp.bfloat16))
                col = col + jnp.where(slot == 0, start_f, 0.0)
                near3[rows(m), :] = col.astype(jnp.bfloat16)

            @pl.when(jnp.logical_not(live))
            def _():
                near3[rows(m), :] = jnp.where(slot == 0, start_b, zero_b)

        acc[...] = zero_f
        for n in range(NB):
            acc[...] += dot(tab[rows(pairs[g, n]), :], near3[rows(n), :])
        col = dot(tw[rows(own), :], acc[...].astype(jnp.bfloat16)) + start_f
        w_real = wts[0, 0]
        w_imag = wts[0, 1]
        green = jnp.concatenate(
            [w_real * col[:L] - w_imag * col[L:], w_real * col[L:] + w_imag * col[:L]], axis=0
        )
        out[g] = green.reshape(out.shape[1:])


def xor_pairs(n, bit):
    return [(i, i ^ bit) for i in range(n)]


def gather_atoms(t_mats, n_axis, later):
    if n_axis & (n_axis - 1):
        return lax.all_gather(t_mats, "atom", axis=1, tiled=True), later
    index = lax.axis_index("atom")
    blocks = t_mats
    bit = 1
    while bit < n_axis:
        other = lax.ppermute(blocks, "atom", xor_pairs(n_axis, bit))
        if bit <= 2:
            other, later[bit - 1] = lax.optimization_barrier((other, later[bit - 1]))
        low = (index & bit) == 0
        blocks = jnp.where(
            low, jnp.concatenate([blocks, other], axis=1), jnp.concatenate([other, blocks], axis=1)
        )
        bit *= 2
    return blocks, later


def sum_energies(x, n_axis):
    if n_axis & (n_axis - 1):
        return lax.psum(x, "energy")
    bit = 1
    while bit < n_axis:
        x = x + lax.ppermute(x, "energy", xor_pairs(n_axis, bit))
        bit *= 2
    return x


def body(axis_sizes, t_mats, struct_table, zone_atoms, zone_size, pair_index, zone_link, weights):
    e_dev, a_dev, block_flat = t_mats.shape
    window, (table, zone_link) = gather_atoms(t_mats, axis_sizes["atom"], [struct_table, zone_link])
    n_atoms = window.shape[1]
    k_tab = struct_table.shape[1]
    tab = real_form(table[0]).reshape(k_tab * 2 * L, 2 * L)
    tw = real_form(window[0]).reshape(n_atoms * 2 * L, 2 * L)
    z_slots = zone_atoms.shape[1]
    reach = jnp.any(zone_link.reshape(a_dev, z_slots, NB) == 0, axis=-1).astype(jnp.int32)
    smem = pl.BlockSpec(memory_space=pltpu.SMEM)
    vmem = pl.BlockSpec(memory_space=pltpu.VMEM)
    blocks = pl.pallas_call(
        zone_kernel,
        out_shape=jax.ShapeDtypeStruct((a_dev, 2 * L * L // 128, 128), jnp.float32),
        in_specs=[smem, smem, smem, smem, smem, smem, vmem, vmem],
        out_specs=vmem,
        scratch_shapes=[
            pltpu.VMEM((a_dev, k_tab * 2 * L, L), jnp.float32),
            pltpu.VMEM((NB * 2 * L, L), jnp.bfloat16),
            pltpu.VMEM((2 * L, L), jnp.float32),
            pltpu.VMEM((a_dev, NB + 1, 2 * L, L), jnp.float32),
            pltpu.SMEM((a_dev, 4, NB * NB + 4), jnp.int32),
        ],
    )(zone_link, pair_index, zone_atoms, zone_size, weights, reach, tab, tw)
    blocks = sum_energies(blocks, axis_sizes["energy"])
    return blocks.reshape(a_dev, 2 * L * L)


def solution(mesh):
    return jax.shard_map(
        functools.partial(body, dict(mesh.shape)),
        mesh=mesh,
        in_specs=(
            P("energy", "atom", None),
            P("energy", None, None),
            P("atom", None),
            P("atom"),
            P("atom", None),
            P("atom", None),
            P("energy", None),
        ),
        out_specs=P("atom", None),
        check_vma=False,
    )
```
